256 devices in a mesh: tm: 16 (over y, x), space: 16 (over z, core).
Axes of the slice: x: 4, y: 4, z: 8, core: 2. Of those that a mesh axis runs over, the one named last changes fastest.
Arguments:
- stored: bfloat16 [16, 288, 128, 128], P('tm', None, 'space'), may hold values from -6 to 6
- snapshot: int32 [16, 256], P('tm'), may hold values from 0 to 287, as said below
- balance_coef: float32 [128, 128], P('space'), may hold values from 0.5 to 2
- sea_mask: int32 [128, 128], P('space'), may hold values 0 or 1
Outputs:
- merged_basis: bfloat16 [256, 3, 128, 128], P('tm', None, 'space')
The draws below stay inside these ranges and needn't reach their ends.
Inputs may be any that keep to these rules, and one draw needn't show every extreme that they name: `snapshot`: the 256 indices of one group are distinct.
All inputs are finite; a program needn't handle non-finite values. No bound on the sum of `sea_mask` on one device may be relied on, other than what follows from the above.
Results may differ from the reference program's by a relative error of at most 0.04.
Values may be sent and summed in bfloat16 or wider, within the bound.
No kernel may reach another device: no remote copies, remote signals or barrier semaphores. Data moves between devices by JAX's collectives and lax.ppermute only.
A program may use at most 64 MiB of HBM per device.

```python
import math
import jax
import jax.numpy as jnp
from jax import lax

MEMBERS = 256
STORE = 288
NY = 128
GROUPS = 16
NX = 128
N_TM = 16


def draw_snapshot(key, part):
    group_keys = jax.random.split(jax.random.fold_in(key, 17), GROUPS)
    orders = jax.vmap(lambda one_key: jax.random.permutation(one_key, STORE))(group_keys)
    return orders[:, :MEMBERS].astype(jnp.int32)


def set_ends(array, rng, least, largest):
    longest = array.shape.index(max(array.shape))
    spots = []
    for shift in (0, 1):
        where = [jax.random.randint(jax.random.fold_in(rng, axis), (), 0, length) for axis, length in enumerate(array.shape)]
        where[longest] = (where[longest] + shift) % array.shape[longest]
        spots.append(tuple(where))
    return array.at[spots[0]].set(least).at[spots[1]].set(largest)


def block_levels(own_key, extent, pieces, least, largest):
    level = 1.0
    for axis_at, parts in pieces:
        steps = jax.random.uniform(jax.random.fold_in(jax.random.fold_in(own_key, 6), axis_at), (parts,), jnp.float32, least / len(pieces), largest / len(pieces))
        level = level * jnp.repeat(jnp.exp(steps), extent[axis_at] // parts).reshape((-1,) + (1,) * (len(extent) - 1 - axis_at))
    return level


def centred(stream_key, dims, deviation, bound, cuts=(), kind=jnp.bfloat16):
    drawn = jax.random.normal(stream_key, dims, jnp.float32) * deviation
    if len(cuts) > 0:
        drawn = block_levels(stream_key, dims, cuts, -0.22, 0.18) * drawn
    return jnp.clip(drawn, min=-bound, max=bound).astype(kind)


def setup_inputs(seed: int = 0) -> dict:
    key_of = jax.random.split(jax.random.key(seed), 5)
    return {
        "stored": centred(key_of[0], (GROUPS, STORE, NX, NY), 1.0, 6.0, ((0, 16), (2, 16))),
        "snapshot": draw_snapshot(jax.random.fold_in(key_of[4], 71), 0),
        "balance_coef": jnp.clip(jnp.exp(math.log(2.0) - 1.3862944 * jax.random.uniform(key_of[2], (NX, NY), jnp.float32) ** block_levels(key_of[2], (NX, NY), ((0, 16),), -0.2, 0.2)), 0.5, 2.0),
        "sea_mask": set_ends((jax.random.randint(key_of[3], (NX, NY), 0, 5) < 4).astype(jnp.int32), jax.random.fold_in(key_of[3], 1), 0, 1),
    }


inv_root2 = 0.7071067811865476

def balance(padded, balance_coef, sea_float):
    center = padded[:, 1:-1, :]
    values = center.astype(jnp.float32)
    east_cells = jnp.roll(values, -1, axis=2)
    west_cells = jnp.roll(values, 1, axis=2)
    zonal_flow = (-balance_coef * sea_float * (east_cells - west_cells)).astype(jnp.bfloat16)
    wide = padded.astype(jnp.float32)
    merid_flow = (balance_coef * sea_float * (wide[:, 2:, :] - wide[:, :-2, :])).astype(jnp.bfloat16)
    return jnp.stack([center, zonal_flow, merid_flow], axis=1).reshape(center.shape[0], -1)

def merge_pair(stacked):
    half_rows = stacked.shape[0] // 2
    gram_full = jnp.dot(stacked.astype(jnp.float32), stacked.T.astype(jnp.float32), preferred_element_type=jnp.float32)
    mixed_cols = (gram_full[:, :half_rows] + gram_full[:, half_rows:]) * inv_root2
    normal = jnp.dot(mixed_cols.T.astype(jnp.float32), mixed_cols.astype(jnp.float32), precision=lax.Precision.HIGHEST, preferred_element_type=jnp.float32)
    factor_low = jnp.linalg.cholesky(normal)
    rotation = (jax.scipy.linalg.solve_triangular(factor_low, mixed_cols.T, lower=True) * inv_root2).astype(jnp.bfloat16)
    return jnp.dot(rotation.astype(jnp.float32), stacked.astype(jnp.float32), preferred_element_type=jnp.float32).astype(jnp.bfloat16)

def reference(stored, snapshot, balance_coef, sea_mask):
    sea_float = sea_mask.astype(jnp.float32)
    mean_state = jnp.mean(stored.astype(jnp.float32), axis=1)
    picked = jax.vmap(lambda states, chosen: jnp.take(states, chosen, axis=0))(stored, snapshot)
    anomaly = ((picked.astype(jnp.float32) - mean_state[:, None]) * sea_float).astype(jnp.bfloat16)
    padded = jnp.pad(anomaly, ((0, 0), (0, 0), (1, 1), (0, 0)))
    bases = jax.vmap(lambda one_group: balance(one_group, balance_coef, sea_float))(padded)
    groups = bases.shape[0]
    width = bases.shape[2]
    levels = N_TM.bit_length() - 1
    for level_idx in range(levels):
        paired = bases.reshape(groups // 2, 2 * MEMBERS, width)
        bases = lax.map(merge_pair, paired)
        groups = groups // 2
    return bases[0].reshape(MEMBERS, 3, NX, NY)
```

```python
import jax
import jax.numpy as jnp
from jax import lax
from jax.sharding import PartitionSpec as P

inv_root2 = 0.7071067811865476


def gathered_total(shard, axis):
    return lax.all_gather(shard, axis).astype(jnp.float32).sum(0)


def with_halo(cells, sides, width):
    for axis, dim in sides:
        count = lax.axis_size(axis)
        ends = count - 1
        head = lax.slice_in_dim(cells, 0, width, axis=dim)
        tail = lax.slice_in_dim(cells, cells.shape[dim] - width, cells.shape[dim], axis=dim)
        cells = jnp.concatenate(
            [
                lax.ppermute(tail, axis, [(i, (i + 1) % count) for i in range(ends)]),
                cells,
                lax.ppermute(head, axis, [((i + 1) % count, i) for i in range(ends)]),
            ],
            axis=dim,
        )
    return cells


def from_partner(shard, axis, stride):
    return lax.ppermute(shard, axis, [(i, i ^ 1 << stride) for i in range(lax.axis_size(axis))])


def balance(padded, balance_coef, sea_float):
    center = padded[:, 1:-1, :]
    values = center.astype(jnp.float32)
    east_cells = jnp.roll(values, -1, axis=2)
    west_cells = jnp.roll(values, 1, axis=2)
    zonal_flow = (-balance_coef * sea_float * (east_cells - west_cells)).astype(jnp.bfloat16)
    wide = padded.astype(jnp.float32)
    merid_flow = (balance_coef * sea_float * (wide[:, 2:, :] - wide[:, :-2, :])).astype(
        jnp.bfloat16
    )
    return jnp.stack([center, zonal_flow, merid_flow], axis=1).reshape(center.shape[0], -1)


def stack_pair(own_basis, other_basis, level_idx):
    own_bit = lax.axis_index("tm") // 2**level_idx % 2
    upper_part = jnp.where(own_bit == 0, own_basis, other_basis)
    lower_part = jnp.where(own_bit == 0, other_basis, own_basis)
    return jnp.concatenate([upper_part, lower_part], axis=0)


def merge_pair(own_basis, other_basis, level_idx, last_level):
    stacked = stack_pair(own_basis, other_basis, level_idx)
    members = own_basis.shape[0]
    local_gram = jnp.dot(stacked, stacked.T, preferred_element_type=jnp.float32)
    local_mixed = (local_gram[:, :members] + local_gram[:, members:]) * inv_root2
    mixed_cols = lax.psum(local_mixed, "space")
    normal = jnp.dot(
        mixed_cols.T,
        mixed_cols,
        precision=lax.Precision.HIGHEST,
        preferred_element_type=jnp.float32,
    )
    factor_low = jnp.linalg.cholesky(normal)
    rotation = (
        jax.scipy.linalg.solve_triangular(factor_low, mixed_cols.T, lower=True) * inv_root2
    ).astype(jnp.bfloat16)
    if last_level:
        member_share = rotation.shape[0] // lax.axis_size("tm")
        rotation = lax.dynamic_slice_in_dim(
            rotation, lax.axis_index("tm") * member_share, member_share, 0
        )
    return jnp.dot(rotation, stacked, preferred_element_type=jnp.float32).astype(jnp.bfloat16)


def body(stored, snapshot, balance_coef, sea_mask):
    sea_float = sea_mask.astype(jnp.float32)
    mean_state = jnp.mean(stored[0].astype(jnp.float32), axis=0)
    picked = jnp.take(stored[0], snapshot[0], axis=0)
    anomaly = ((picked.astype(jnp.float32) - mean_state) * sea_float).astype(jnp.bfloat16)
    padded = with_halo(anomaly, (("space", 1),), 1)
    basis_now = balance(padded, balance_coef, sea_float)
    levels = lax.axis_size("tm").bit_length() - 1
    first_level = 0
    other_padded = from_partner(padded, "tm", 0)
    partner = balance(other_padded, balance_coef, sea_float)
    basis_now = merge_pair(basis_now, partner, 0, levels == 1)
    first_level = 1
    for level_idx in range(first_level, levels):
        partner = from_partner(basis_now, "tm", level_idx)
        basis_now = merge_pair(basis_now, partner, level_idx, level_idx == levels - 1)
    return basis_now.reshape(basis_now.shape[0], 3, stored.shape[2], stored.shape[3])


def solution(mesh):
    placed = (P("tm", None, "space", None), P("tm", None), P("space", None), P("space", None))
    return jax.shard_map(
        body, mesh=mesh, in_specs=placed, out_specs=P("tm", None, "space", None), check_vma=False
    )
```

```python
import jax
import jax.numpy as jnp
from jax import lax
from jax.sharding import PartitionSpec as P

inv_root2 = 0.7071067811865476


def gathered_total(shard, axis):
    return lax.all_gather(shard, axis).astype(jnp.float32).sum(0)


def summed_rows(shard, axis):
    count = lax.axis_size(axis)
    parts = lax.all_to_all(shard, axis, 0, 0, tiled=True)
    parts = parts.reshape(count, shard.shape[0] // count, shard.shape[1])
    own_rows = parts.astype(jnp.float32).sum(0)
    return lax.all_gather(own_rows, axis, axis=0, tiled=True)


def with_halo(cells, sides, width):
    for axis, dim in sides:
        count = lax.axis_size(axis)
        ends = count - 1
        head = lax.slice_in_dim(cells, 0, width, axis=dim)
        tail = lax.slice_in_dim(cells, cells.shape[dim] - width, cells.shape[dim], axis=dim)
        cells = jnp.concatenate(
            [
                lax.ppermute(tail, axis, [(i, (i + 1) % count) for i in range(ends)]),
                cells,
                lax.ppermute(head, axis, [((i + 1) % count, i) for i in range(ends)]),
            ],
            axis=dim,
        )
    return cells


def from_partner(shard, axis, stride):
    return lax.ppermute(shard, axis, [(i, i ^ 1 << stride) for i in range(lax.axis_size(axis))])


def balance(padded, balance_coef, sea_float):
    center = padded[:, 1:-1, :]
    values = center.astype(jnp.float32)
    east_cells = jnp.roll(values, -1, axis=2)
    west_cells = jnp.roll(values, 1, axis=2)
    zonal_flow = (-balance_coef * sea_float * (east_cells - west_cells)).astype(jnp.bfloat16)
    wide = padded.astype(jnp.float32)
    merid_flow = (balance_coef * sea_float * (wide[:, 2:, :] - wide[:, :-2, :])).astype(
        jnp.bfloat16
    )
    return jnp.stack([center, zonal_flow, merid_flow], axis=1).reshape(center.shape[0], -1)


def stack_pair(own_basis, other_basis, level_idx):
    own_bit = lax.axis_index("tm") // 2**level_idx % 2
    upper_part = jnp.where(own_bit == 0, own_basis, other_basis)
    lower_part = jnp.where(own_bit == 0, other_basis, own_basis)
    return jnp.concatenate([upper_part, lower_part], axis=0)


def merge_pair(own_basis, other_basis, level_idx, last_level):
    stacked = stack_pair(own_basis, other_basis, level_idx)
    members = own_basis.shape[0]
    local_gram = jnp.dot(stacked, stacked.T, preferred_element_type=jnp.float32)
    local_mixed = (local_gram[:, :members] + local_gram[:, members:]) * inv_root2
    mixed_cols = summed_rows(local_mixed.astype(jnp.bfloat16), "space")
    normal = jnp.dot(
        mixed_cols.T,
        mixed_cols,
        precision=lax.Precision.HIGHEST,
        preferred_element_type=jnp.float32,
    )
    factor_low = jnp.linalg.cholesky(normal)
    rotation = (
        jax.scipy.linalg.solve_triangular(factor_low, mixed_cols.T, lower=True) * inv_root2
    ).astype(jnp.bfloat16)
    if last_level:
        member_share = rotation.shape[0] // lax.axis_size("tm")
        rotation = lax.dynamic_slice_in_dim(
            rotation, lax.axis_index("tm") * member_share, member_share, 0
        )
    return jnp.dot(rotation, stacked, preferred_element_type=jnp.float32).astype(jnp.bfloat16)


def body(stored, snapshot, balance_coef, sea_mask):
    sea_float = sea_mask.astype(jnp.float32)
    mean_state = jnp.mean(stored[0].astype(jnp.float32), axis=0)
    picked = jnp.take(stored[0], snapshot[0], axis=0)
    anomaly = ((picked.astype(jnp.float32) - mean_state) * sea_float).astype(jnp.bfloat16)
    padded = with_halo(anomaly, (("space", 1),), 1)
    basis_now = balance(padded, balance_coef, sea_float)
    levels = lax.axis_size("tm").bit_length() - 1
    first_level = 0
    other_padded = from_partner(padded, "tm", 0)
    partner = balance(other_padded, balance_coef, sea_float)
    basis_now = merge_pair(basis_now, partner, 0, levels == 1)
    first_level = 1
    for level_idx in range(first_level, levels):
        partner = from_partner(basis_now, "tm", level_idx)
        basis_now = merge_pair(basis_now, partner, level_idx, level_idx == levels - 1)
    return basis_now.reshape(basis_now.shape[0], 3, stored.shape[2], stored.shape[3])


def solution(mesh):
    placed = (P("tm", None, "space", None), P("tm", None), P("space", None), P("space", None))
    return jax.shard_map(
        body, mesh=mesh, in_specs=placed, out_specs=P("tm", None, "space", None), check_vma=False
    )
```

```python
import jax
import jax.numpy as jnp
from jax import lax
from jax.sharding import PartitionSpec as P

inv_root2 = 0.7071067811865476


def gathered_total(shard, axis):
    return lax.all_gather(shard, axis).astype(jnp.float32).sum(0)


def summed_rows(shard, axis):
    count = lax.axis_size(axis)
    parts = lax.all_to_all(shard, axis, 0, 0, tiled=True)
    parts = parts.reshape(count, shard.shape[0] // count, shard.shape[1])
    own_rows = parts.astype(jnp.float32).sum(0)
    return lax.all_gather(own_rows, axis, axis=0, tiled=True)


def with_halo(cells, sides, width):
    for axis, dim in sides:
        count = lax.axis_size(axis)
        ends = count - 1
        head = lax.slice_in_dim(cells, 0, width, axis=dim)
        tail = lax.slice_in_dim(cells, cells.shape[dim] - width, cells.shape[dim], axis=dim)
        cells = jnp.concatenate(
            [
                lax.ppermute(tail, axis, [(i, (i + 1) % count) for i in range(ends)]),
                cells,
                lax.ppermute(head, axis, [((i + 1) % count, i) for i in range(ends)]),
            ],
            axis=dim,
        )
    return cells


def from_partner(shard, axis, stride):
    return lax.ppermute(shard, axis, [(i, i ^ 1 << stride) for i in range(lax.axis_size(axis))])


def balance(padded, balance_coef, sea_float):
    center = padded[:, 1:-1, :]
    values = center.astype(jnp.float32)
    east_cells = jnp.roll(values, -1, axis=2)
    west_cells = jnp.roll(values, 1, axis=2)
    zonal_flow = (-balance_coef * sea_float * (east_cells - west_cells)).astype(jnp.bfloat16)
    wide = padded.astype(jnp.float32)
    merid_flow = (balance_coef * sea_float * (wide[:, 2:, :] - wide[:, :-2, :])).astype(
        jnp.bfloat16
    )
    return jnp.stack([center, zonal_flow, merid_flow], axis=1).reshape(center.shape[0], -1)


def stack_pair(own_basis, other_basis, level_idx):
    own_bit = lax.axis_index("tm") // 2**level_idx % 2
    upper_part = jnp.where(own_bit == 0, own_basis, other_basis)
    lower_part = jnp.where(own_bit == 0, other_basis, own_basis)
    return jnp.concatenate([upper_part, lower_part], axis=0)


def rotation_of(stacked):
    members = stacked.shape[0] // 2
    local_gram = jnp.dot(stacked, stacked.T, preferred_element_type=jnp.float32)
    local_mixed = (local_gram[:, :members] + local_gram[:, members:]) * inv_root2
    mixed_cols = summed_rows(local_mixed.astype(jnp.bfloat16), "space")
    normal = jnp.dot(
        mixed_cols.T,
        mixed_cols,
        precision=lax.Precision.HIGHEST,
        preferred_element_type=jnp.float32,
    )
    factor_low = jnp.linalg.cholesky(normal)
    return (
        jax.scipy.linalg.solve_triangular(factor_low, mixed_cols.T, lower=True) * inv_root2
    ).astype(jnp.bfloat16)


def rotated(rotation, stacked):
    return jnp.dot(rotation, stacked, preferred_element_type=jnp.float32).astype(jnp.bfloat16)


def body(stored, snapshot, balance_coef, sea_mask):
    sea_float = sea_mask.astype(jnp.float32)
    mean_state = jnp.mean(stored[0].astype(jnp.float32), axis=0)
    picked = jnp.take(stored[0], snapshot[0], axis=0)
    anomaly = ((picked.astype(jnp.float32) - mean_state) * sea_float).astype(jnp.bfloat16)
    padded = with_halo(anomaly, (("space", 1),), 1)
    basis_now = balance(padded, balance_coef, sea_float)
    levels = lax.axis_size("tm").bit_length() - 1
    other_padded = from_partner(padded, "tm", 0)
    partner = balance(other_padded, balance_coef, sea_float)
    stacked = stack_pair(basis_now, partner, 0)
    for level_idx in range(levels):
        if level_idx == levels - 1:
            rotation = rotation_of(stacked)
            member_share = rotation.shape[0] // lax.axis_size("tm")
            rotation = lax.dynamic_slice_in_dim(
                rotation, lax.axis_index("tm") * member_share, member_share, 0
            )
            basis_now = rotated(rotation, stacked)
        else:
            partner_stacked = from_partner(stacked, "tm", level_idx + 1)
            rotation = rotation_of(stacked)
            partner_rotation = from_partner(rotation, "tm", level_idx + 1)
            basis_now = rotated(rotation, stacked)
            partner = rotated(partner_rotation, partner_stacked)
            stacked = stack_pair(basis_now, partner, level_idx + 1)
    return basis_now.reshape(basis_now.shape[0], 3, stored.shape[2], stored.shape[3])


def solution(mesh):
    placed = (P("tm", None, "space", None), P("tm", None), P("space", None), P("space", None))
    return jax.shard_map(
        body, mesh=mesh, in_specs=placed, out_specs=P("tm", None, "space", None), check_vma=False
    )
```

```python
import jax
import jax.numpy as jnp
from jax import lax
from jax.sharding import PartitionSpec as P

inv_root2 = 0.7071067811865476


def gathered_total(shard, axis):
    return lax.all_gather(shard, axis).astype(jnp.float32).sum(0)


def summed_rows(shard, axis):
    count = lax.axis_size(axis)
    parts = lax.all_to_all(shard, axis, 0, 0, tiled=True)
    parts = parts.reshape(count, shard.shape[0] // count, shard.shape[1])
    own_rows = parts.astype(jnp.float32).sum(0)
    return lax.all_gather(own_rows, axis, axis=0, tiled=True)


def with_halo(cells, sides, width):
    for axis, dim in sides:
        count = lax.axis_size(axis)
        ends = count - 1
        head = lax.slice_in_dim(cells, 0, width, axis=dim)
        tail = lax.slice_in_dim(cells, cells.shape[dim] - width, cells.shape[dim], axis=dim)
        cells = jnp.concatenate(
            [
                lax.ppermute(tail, axis, [(i, (i + 1) % count) for i in range(ends)]),
                cells,
                lax.ppermute(head, axis, [((i + 1) % count, i) for i in range(ends)]),
            ],
            axis=dim,
        )
    return cells


def from_partner(shard, axis, stride):
    return lax.ppermute(shard, axis, [(i, i ^ 1 << stride) for i in range(lax.axis_size(axis))])


def balance(padded, balance_coef, sea_float):
    center = padded[:, 1:-1, :]
    values = center.astype(jnp.float32)
    east_cells = jnp.roll(values, -1, axis=2)
    west_cells = jnp.roll(values, 1, axis=2)
    zonal_flow = (-balance_coef * sea_float * (east_cells - west_cells)).astype(jnp.bfloat16)
    wide = padded.astype(jnp.float32)
    merid_flow = (balance_coef * sea_float * (wide[:, 2:, :] - wide[:, :-2, :])).astype(
        jnp.bfloat16
    )
    return jnp.stack([center, zonal_flow, merid_flow], axis=1).reshape(center.shape[0], -1)


def stack_pair(own_basis, other_basis, level_idx):
    own_bit = lax.axis_index("tm") // 2**level_idx % 2
    upper_part = jnp.where(own_bit == 0, own_basis, other_basis)
    lower_part = jnp.where(own_bit == 0, other_basis, own_basis)
    return jnp.concatenate([upper_part, lower_part], axis=0)


def rotation_of(stacked):
    members = stacked.shape[0] // 2
    local_gram = jnp.dot(stacked, stacked.T, preferred_element_type=jnp.float32)
    local_mixed = (local_gram[:, :members] + local_gram[:, members:]) * inv_root2
    mixed_cols = summed_rows(local_mixed.astype(jnp.bfloat16), "space")
    normal = jnp.dot(
        mixed_cols.T,
        mixed_cols,
        precision=lax.Precision.HIGHEST,
        preferred_element_type=jnp.float32,
    )
    half = normal.shape[0] // 2
    low_11 = jnp.linalg.cholesky(normal[:half, :half])
    low_21 = lax.linalg.triangular_solve(
        low_11, normal[half:, :half], left_side=False, lower=True, transpose_a=True
    )
    low_22 = jnp.linalg.cholesky(normal[half:, half:] - highest_dot(low_21, low_21.T))
    upper_rows = jax.scipy.linalg.solve_triangular(low_11, mixed_cols[:, :half].T, lower=True)
    lower_rows = jax.scipy.linalg.solve_triangular(
        low_22, mixed_cols[:, half:].T - highest_dot(low_21, upper_rows), lower=True
    )
    return (jnp.concatenate([upper_rows, lower_rows], axis=0) * inv_root2).astype(jnp.bfloat16)


def highest_dot(left, right):
    return jnp.dot(
        left, right, precision=lax.Precision.HIGHEST, preferred_element_type=jnp.float32
    )


def rotated(rotation, stacked):
    return jnp.dot(rotation, stacked, preferred_element_type=jnp.float32).astype(jnp.bfloat16)


def body(stored, snapshot, balance_coef, sea_mask):
    sea_float = sea_mask.astype(jnp.float32)
    mean_state = jnp.mean(stored[0].astype(jnp.float32), axis=0)
    picked = jnp.take(stored[0], snapshot[0], axis=0)
    anomaly = ((picked.astype(jnp.float32) - mean_state) * sea_float).astype(jnp.bfloat16)
    padded = with_halo(anomaly, (("space", 1),), 1)
    basis_now = balance(padded, balance_coef, sea_float)
    levels = lax.axis_size("tm").bit_length() - 1
    other_padded = from_partner(padded, "tm", 0)
    partner = balance(other_padded, balance_coef, sea_float)
    stacked = stack_pair(basis_now, partner, 0)
    for level_idx in range(levels):
        if level_idx == levels - 1:
            rotation = rotation_of(stacked)
            member_share = rotation.shape[0] // lax.axis_size("tm")
            rotation = lax.dynamic_slice_in_dim(
                rotation, lax.axis_index("tm") * member_share, member_share, 0
            )
            basis_now = rotated(rotation, stacked)
        else:
            partner_stacked = from_partner(stacked, "tm", level_idx + 1)
            rotation = rotation_of(stacked)
            partner_rotation = from_partner(rotation, "tm", level_idx + 1)
            basis_now = rotated(rotation, stacked)
            partner = rotated(partner_rotation, partner_stacked)
            stacked = stack_pair(basis_now, partner, level_idx + 1)
    return basis_now.reshape(basis_now.shape[0], 3, stored.shape[2], stored.shape[3])


def solution(mesh):
    placed = (P("tm", None, "space", None), P("tm", None), P("space", None), P("space", None))
    return jax.shard_map(
        body, mesh=mesh, in_specs=placed, out_specs=P("tm", None, "space", None), check_vma=False
    )
```

```python
import jax
import jax.numpy as jnp
from jax import lax
from jax.sharding import PartitionSpec as P

inv_root2 = 0.7071067811865476


def gathered_total(shard, axis):
    return lax.all_gather(shard, axis).astype(jnp.float32).sum(0)


def summed_rows(shard, axis):
    count = lax.axis_size(axis)
    parts = lax.all_to_all(shard, axis, 0, 0, tiled=True)
    parts = parts.reshape(count, shard.shape[0] // count, shard.shape[1])
    own_rows = parts.astype(jnp.float32).sum(0)
    return lax.all_gather(own_rows, axis, axis=0, tiled=True)


def with_halo(cells, sides, width):
    for axis, dim in sides:
        count = lax.axis_size(axis)
        ends = count - 1
        head = lax.slice_in_dim(cells, 0, width, axis=dim)
        tail = lax.slice_in_dim(cells, cells.shape[dim] - width, cells.shape[dim], axis=dim)
        cells = jnp.concatenate(
            [
                lax.ppermute(tail, axis, [(i, (i + 1) % count) for i in range(ends)]),
                cells,
                lax.ppermute(head, axis, [((i + 1) % count, i) for i in range(ends)]),
            ],
            axis=dim,
        )
    return cells


def from_partner(shard, axis, stride):
    return lax.ppermute(shard, axis, [(i, i ^ 1 << stride) for i in range(lax.axis_size(axis))])


def balance(padded, balance_coef, sea_float):
    center = padded[:, 1:-1, :]
    values = center.astype(jnp.float32)
    east_cells = jnp.roll(values, -1, axis=2)
    west_cells = jnp.roll(values, 1, axis=2)
    zonal_flow = (-balance_coef * sea_float * (east_cells - west_cells)).astype(jnp.bfloat16)
    wide = padded.astype(jnp.float32)
    merid_flow = (balance_coef * sea_float * (wide[:, 2:, :] - wide[:, :-2, :])).astype(
        jnp.bfloat16
    )
    return jnp.stack([center, zonal_flow, merid_flow], axis=1).reshape(center.shape[0], -1)


def stack_pair(own_basis, other_basis):
    return jnp.concatenate([own_basis, other_basis], axis=0)


def rotation_of(stacked):
    members = stacked.shape[0] // 2
    local_gram = jnp.dot(stacked, stacked.T, preferred_element_type=jnp.float32)
    local_mixed = (local_gram[:, :members] + local_gram[:, members:]) * inv_root2
    mixed_cols = summed_rows(local_mixed.astype(jnp.bfloat16), "space")
    normal = jnp.dot(
        mixed_cols.T,
        mixed_cols,
        precision=lax.Precision.HIGHEST,
        preferred_element_type=jnp.float32,
    )
    half = normal.shape[0] // 2
    low_11 = jnp.linalg.cholesky(normal[:half, :half])
    low_21 = lax.linalg.triangular_solve(
        low_11, normal[half:, :half], left_side=False, lower=True, transpose_a=True
    )
    low_22 = jnp.linalg.cholesky(normal[half:, half:] - highest_dot(low_21, low_21.T))
    upper_rows = jax.scipy.linalg.solve_triangular(low_11, mixed_cols[:, :half].T, lower=True)
    lower_rows = jax.scipy.linalg.solve_triangular(
        low_22, mixed_cols[:, half:].T - highest_dot(low_21, upper_rows), lower=True
    )
    return (jnp.concatenate([upper_rows, lower_rows], axis=0) * inv_root2).astype(jnp.bfloat16)


def highest_dot(left, right):
    return jnp.dot(
        left, right, precision=lax.Precision.HIGHEST, preferred_element_type=jnp.float32
    )


def rotated(rotation, stacked):
    return jnp.dot(rotation, stacked, preferred_element_type=jnp.float32).astype(jnp.bfloat16)


def body(stored, snapshot, balance_coef, sea_mask):
    sea_float = sea_mask.astype(jnp.float32)
    mean_state = jnp.mean(stored[0].astype(jnp.float32), axis=0)
    picked = jnp.take(stored[0], snapshot[0], axis=0)
    anomaly = ((picked.astype(jnp.float32) - mean_state) * sea_float).astype(jnp.bfloat16)
    padded = with_halo(anomaly, (("space", 1),), 1)
    basis_now = balance(padded, balance_coef, sea_float)
    levels = lax.axis_size("tm").bit_length() - 1
    other_padded = from_partner(padded, "tm", 0)
    partner = balance(other_padded, balance_coef, sea_float)
    stacked = stack_pair(basis_now, partner)
    for level_idx in range(levels):
        if level_idx == levels - 1:
            rotation = rotation_of(stacked)
            member_share = rotation.shape[0] // lax.axis_size("tm")
            rotation = lax.dynamic_slice_in_dim(
                rotation, lax.axis_index("tm") * member_share, member_share, 0
            )
            basis_now = rotated(rotation, stacked)
        else:
            partner_stacked = from_partner(stacked, "tm", level_idx + 1)
            rotation = rotation_of(stacked)
            partner_rotation = from_partner(rotation, "tm", level_idx + 1)
            basis_now = rotated(rotation, stacked)
            partner = rotated(partner_rotation, partner_stacked)
            stacked = stack_pair(basis_now, partner)
    return basis_now.reshape(basis_now.shape[0], 3, stored.shape[2], stored.shape[3])


def solution(mesh):
    placed = (P("tm", None, "space", None), P("tm", None), P("space", None), P("space", None))
    return jax.shard_map(
        body, mesh=mesh, in_specs=placed, out_specs=P("tm", None, "space", None), check_vma=False
    )
```

```python
import jax
import jax.numpy as jnp
from jax import lax
from jax.sharding import PartitionSpec as P

inv_root2 = 0.7071067811865476


def gathered_total(shard, axis):
    return lax.all_gather(shard, axis).astype(jnp.float32).sum(0)


def summed_rows(shard, axis):
    count = lax.axis_size(axis)
    parts = lax.all_to_all(shard, axis, 0, 0, tiled=True)
    parts = parts.reshape(count, shard.shape[0] // count, shard.shape[1])
    own_rows = parts.astype(jnp.float32).sum(0)
    return lax.all_to_all(jnp.tile(own_rows, (count, 1)), axis, 0, 0, tiled=True)


def with_halo(cells, sides, width):
    for axis, dim in sides:
        count = lax.axis_size(axis)
        ends = count - 1
        head = lax.slice_in_dim(cells, 0, width, axis=dim)
        tail = lax.slice_in_dim(cells, cells.shape[dim] - width, cells.shape[dim], axis=dim)
        cells = jnp.concatenate(
            [
                lax.ppermute(tail, axis, [(i, (i + 1) % count) for i in range(ends)]),
                cells,
                lax.ppermute(head, axis, [((i + 1) % count, i) for i in range(ends)]),
            ],
            axis=dim,
        )
    return cells


def from_partner(shard, axis, stride):
    return lax.ppermute(shard, axis, [(i, i ^ 1 << stride) for i in range(lax.axis_size(axis))])


def balance(padded, balance_coef, sea_float):
    center = padded[:, 1:-1, :]
    values = center.astype(jnp.float32)
    east_cells = jnp.roll(values, -1, axis=2)
    west_cells = jnp.roll(values, 1, axis=2)
    zonal_flow = (-balance_coef * sea_float * (east_cells - west_cells)).astype(jnp.bfloat16)
    wide = padded.astype(jnp.float32)
    merid_flow = (balance_coef * sea_float * (wide[:, 2:, :] - wide[:, :-2, :])).astype(
        jnp.bfloat16
    )
    return jnp.stack([center, zonal_flow, merid_flow], axis=1).reshape(center.shape[0], -1)


def stack_pair(own_basis, other_basis):
    return jnp.concatenate([own_basis, other_basis], axis=0)


def rotation_of(stacked):
    members = stacked.shape[0] // 2
    half = members // 2
    local_gram = jnp.dot(stacked, stacked.T, preferred_element_type=jnp.float32)
    local_mixed = ((local_gram[:, :members] + local_gram[:, members:]) * inv_root2).astype(
        jnp.bfloat16
    )
    mixed_left = summed_rows(local_mixed[:, :half], "space")
    mixed_right = summed_rows(local_mixed[:, half:], "space")
    low_11 = jnp.linalg.cholesky(highest_dot(mixed_left.T, mixed_left))
    low_21 = lax.linalg.triangular_solve(
        low_11, highest_dot(mixed_right.T, mixed_left), left_side=False, lower=True, transpose_a=True
    )
    low_22 = jnp.linalg.cholesky(
        highest_dot(mixed_right.T, mixed_right) - highest_dot(low_21, low_21.T)
    )
    upper_rows = jax.scipy.linalg.solve_triangular(low_11, mixed_left.T, lower=True)
    lower_rows = jax.scipy.linalg.solve_triangular(
        low_22, mixed_right.T - highest_dot(low_21, upper_rows), lower=True
    )
    return (jnp.concatenate([upper_rows, lower_rows], axis=0) * inv_root2).astype(jnp.bfloat16)


def highest_dot(left, right):
    return jnp.dot(
        left, right, precision=lax.Precision.HIGHEST, preferred_element_type=jnp.float32
    )


def rotated(rotation, stacked):
    return jnp.dot(rotation, stacked, preferred_element_type=jnp.float32).astype(jnp.bfloat16)


def body(stored, snapshot, balance_coef, sea_mask):
    sea_float = sea_mask.astype(jnp.float32)
    mean_state = jnp.mean(stored[0].astype(jnp.float32), axis=0)
    picked = jnp.take(stored[0], snapshot[0], axis=0)
    anomaly = ((picked.astype(jnp.float32) - mean_state) * sea_float).astype(jnp.bfloat16)
    padded = with_halo(anomaly, (("space", 1),), 1)
    basis_now = balance(padded, balance_coef, sea_float)
    levels = lax.axis_size("tm").bit_length() - 1
    other_padded = from_partner(padded, "tm", 0)
    partner = balance(other_padded, balance_coef, sea_float)
    stacked = stack_pair(basis_now, partner)
    for level_idx in range(levels):
        if level_idx == levels - 1:
            rotation = rotation_of(stacked)
            member_share = rotation.shape[0] // lax.axis_size("tm")
            rotation = lax.dynamic_slice_in_dim(
                rotation, lax.axis_index("tm") * member_share, member_share, 0
            )
            basis_now = rotated(rotation, stacked)
        else:
            partner_stacked = from_partner(stacked, "tm", level_idx + 1)
            rotation = rotation_of(stacked)
            partner_rotation = from_partner(rotation, "tm", level_idx + 1)
            basis_now = rotated(rotation, stacked)
            partner = rotated(partner_rotation, partner_stacked)
            stacked = stack_pair(basis_now, partner)
    return basis_now.reshape(basis_now.shape[0], 3, stored.shape[2], stored.shape[3])


def solution(mesh):
    placed = (P("tm", None, "space", None), P("tm", None), P("space", None), P("space", None))
    return jax.shard_map(
        body, mesh=mesh, in_specs=placed, out_specs=P("tm", None, "space", None), check_vma=False
    )
```

```python
import jax
import jax.numpy as jnp
from jax import lax
from jax.sharding import PartitionSpec as P

inv_root2 = 0.7071067811865476


def gathered_total(shard, axis):
    return lax.all_gather(shard, axis).astype(jnp.float32).sum(0)


def summed_rows(shard, axis):
    count = lax.axis_size(axis)
    parts = lax.all_to_all(shard, axis, 0, 0, tiled=True)
    parts = parts.reshape(count, shard.shape[0] // count, shard.shape[1])
    own_rows = parts.astype(jnp.float32).sum(0)
    return lax.all_gather(own_rows, axis, axis=0, tiled=True)


def with_halo(cells, sides, width):
    for axis, dim in sides:
        count = lax.axis_size(axis)
        ends = count - 1
        head = lax.slice_in_dim(cells, 0, width, axis=dim)
        tail = lax.slice_in_dim(cells, cells.shape[dim] - width, cells.shape[dim], axis=dim)
        cells = jnp.concatenate(
            [
                lax.ppermute(tail, axis, [(i, (i + 1) % count) for i in range(ends)]),
                cells,
                lax.ppermute(head, axis, [((i + 1) % count, i) for i in range(ends)]),
            ],
            axis=dim,
        )
    return cells


def from_partner(shard, axis, stride):
    return lax.ppermute(shard, axis, [(i, i ^ 1 << stride) for i in range(lax.axis_size(axis))])


def balance(padded, balance_coef, sea_float):
    center = padded[:, 1:-1, :]
    cells = lax.broadcasted_iota(jnp.int32, (center.shape[2], center.shape[2]), 0)
    targets = lax.broadcasted_iota(jnp.int32, (center.shape[2], center.shape[2]), 1)
    count = center.shape[2]
    circulant = (cells == (targets + 1) % count).astype(jnp.bfloat16) - (
        cells == (targets - 1) % count
    ).astype(jnp.bfloat16)
    east_minus_west = jnp.einsum(
        "mxy,yz->mxz", center, circulant, preferred_element_type=jnp.float32
    )
    zonal_flow = (-balance_coef * sea_float * east_minus_west).astype(jnp.bfloat16)
    wide = padded.astype(jnp.float32)
    merid_flow = (balance_coef * sea_float * (wide[:, 2:, :] - wide[:, :-2, :])).astype(
        jnp.bfloat16
    )
    return jnp.stack([center, zonal_flow, merid_flow], axis=1).reshape(center.shape[0], -1)


def stack_pair(own_basis, other_basis):
    return jnp.concatenate([own_basis, other_basis], axis=0)


def rotation_of(stacked):
    members = stacked.shape[0] // 2
    local_gram = jnp.dot(stacked, stacked.T, preferred_element_type=jnp.float32)
    local_mixed = (local_gram[:, :members] + local_gram[:, members:]) * inv_root2
    mixed_cols = summed_rows(local_mixed.astype(jnp.bfloat16), "space")
    normal = jnp.dot(
        mixed_cols.T,
        mixed_cols,
        precision=lax.Precision.HIGHEST,
        preferred_element_type=jnp.float32,
    )
    half = normal.shape[0] // 2
    low_11 = jnp.linalg.cholesky(normal[:half, :half])
    low_21 = lax.linalg.triangular_solve(
        low_11, normal[half:, :half], left_side=False, lower=True, transpose_a=True
    )
    low_22 = jnp.linalg.cholesky(normal[half:, half:] - highest_dot(low_21, low_21.T))
    upper_rows = jax.scipy.linalg.solve_triangular(low_11, mixed_cols[:, :half].T, lower=True)
    lower_rows = jax.scipy.linalg.solve_triangular(
        low_22, mixed_cols[:, half:].T - highest_dot(low_21, upper_rows), lower=True
    )
    return (jnp.concatenate([upper_rows, lower_rows], axis=0) * inv_root2).astype(jnp.bfloat16)


def highest_dot(left, right):
    return jnp.dot(
        left, right, precision=lax.Precision.HIGHEST, preferred_element_type=jnp.float32
    )


def rotated(rotation, stacked):
    return jnp.dot(rotation, stacked, preferred_element_type=jnp.float32).astype(jnp.bfloat16)


def body(stored, snapshot, balance_coef, sea_mask):
    sea_float = sea_mask.astype(jnp.float32)
    mean_state = jnp.mean(stored[0].astype(jnp.float32), axis=0)
    picked = jnp.take(stored[0], snapshot[0], axis=0)
    anomaly = ((picked.astype(jnp.float32) - mean_state) * sea_float).astype(jnp.bfloat16)
    padded = with_halo(anomaly, (("space", 1),), 1)
    basis_now = balance(padded, balance_coef, sea_float)
    levels = lax.axis_size("tm").bit_length() - 1
    other_padded = from_partner(padded, "tm", 0)
    partner = balance(other_padded, balance_coef, sea_float)
    stacked = stack_pair(basis_now, partner)
    for level_idx in range(levels):
        if level_idx == levels - 1:
            rotation = rotation_of(stacked)
            member_share = rotation.shape[0] // lax.axis_size("tm")
            rotation = lax.dynamic_slice_in_dim(
                rotation, lax.axis_index("tm") * member_share, member_share, 0
            )
            basis_now = rotated(rotation, stacked)
        else:
            partner_stacked = from_partner(stacked, "tm", level_idx + 1)
            rotation = rotation_of(stacked)
            partner_rotation = from_partner(rotation, "tm", level_idx + 1)
            basis_now = rotated(rotation, stacked)
            partner = rotated(partner_rotation, partner_stacked)
            stacked = stack_pair(basis_now, partner)
    return basis_now.reshape(basis_now.shape[0], 3, stored.shape[2], stored.shape[3])


def solution(mesh):
    placed = (P("tm", None, "space", None), P("tm", None), P("space", None), P("space", None))
    return jax.shard_map(
        body, mesh=mesh, in_specs=placed, out_specs=P("tm", None, "space", None), check_vma=False
    )
```

```python
import jax
import jax.numpy as jnp
from jax import lax
from jax.sharding import PartitionSpec as P

inv_root2 = 0.7071067811865476


def gathered_total(shard, axis):
    return lax.all_gather(shard, axis).astype(jnp.float32).sum(0)


def summed_rows(shard, axis):
    count = lax.axis_size(axis)
    parts = lax.all_to_all(shard, axis, 0, 0, tiled=True)
    parts = parts.reshape(count, shard.shape[0] // count, shard.shape[1])
    own_rows = parts.astype(jnp.float32).sum(0)
    return lax.all_gather(own_rows, axis, axis=0, tiled=True)


def with_halo(cells, sides, width):
    for axis, dim in sides:
        count = lax.axis_size(axis)
        ends = count - 1
        head = lax.slice_in_dim(cells, 0, width, axis=dim)
        tail = lax.slice_in_dim(cells, cells.shape[dim] - width, cells.shape[dim], axis=dim)
        cells = jnp.concatenate(
            [
                lax.ppermute(tail, axis, [(i, (i + 1) % count) for i in range(ends)]),
                cells,
                lax.ppermute(head, axis, [((i + 1) % count, i) for i in range(ends)]),
            ],
            axis=dim,
        )
    return cells


def from_partner(shard, axis, stride):
    return lax.ppermute(shard, axis, [(i, i ^ 1 << stride) for i in range(lax.axis_size(axis))])


def balance(padded, balance_coef, sea_float):
    center = padded[:, 1:-1, :]
    cells = lax.broadcasted_iota(jnp.int32, (center.shape[2], center.shape[2]), 0)
    targets = lax.broadcasted_iota(jnp.int32, (center.shape[2], center.shape[2]), 1)
    count = center.shape[2]
    circulant = (cells == (targets + 1) % count).astype(jnp.bfloat16) - (
        cells == (targets - 1) % count
    ).astype(jnp.bfloat16)
    east_minus_west = jnp.einsum(
        "mxy,yz->mxz", center, circulant, preferred_element_type=jnp.float32
    )
    zonal_flow = (-balance_coef * sea_float * east_minus_west).astype(jnp.bfloat16)
    wide = padded.astype(jnp.float32)
    merid_flow = (balance_coef * sea_float * (wide[:, 2:, :] - wide[:, :-2, :])).astype(
        jnp.bfloat16
    )
    return jnp.stack([center, zonal_flow, merid_flow], axis=1).reshape(center.shape[0], -1)


def stack_pair(own_basis, other_basis):
    return jnp.concatenate([own_basis, other_basis], axis=0)


def rotation_of(stacked):
    members = stacked.shape[0] // 2
    local_gram = jnp.dot(stacked, stacked.T, preferred_element_type=jnp.float32)
    local_mixed = (local_gram[:, :members] + local_gram[:, members:]) * inv_root2
    mixed_cols = summed_rows(local_mixed.astype(jnp.bfloat16), "space")
    normal = jnp.dot(
        mixed_cols.T,
        mixed_cols,
        precision=lax.Precision.HIGHEST,
        preferred_element_type=jnp.float32,
    )
    half = normal.shape[0] // 2
    low_11 = jnp.linalg.cholesky(normal[:half, :half])
    low_21 = lax.linalg.triangular_solve(
        low_11, normal[half:, :half], left_side=False, lower=True, transpose_a=True
    )
    low_22 = jnp.linalg.cholesky(normal[half:, half:] - highest_dot(low_21, low_21.T))
    upper_rows = jax.scipy.linalg.solve_triangular(low_11, mixed_cols[:, :half].T, lower=True)
    lower_rows = jax.scipy.linalg.solve_triangular(
        low_22, mixed_cols[:, half:].T - highest_dot(low_21, upper_rows), lower=True
    )
    return (jnp.concatenate([upper_rows, lower_rows], axis=0) * inv_root2).astype(jnp.bfloat16)


def highest_dot(left, right):
    return jnp.dot(
        left, right, precision=lax.Precision.HIGHEST, preferred_element_type=jnp.float32
    )


def rotated(rotation, stacked):
    return jnp.dot(rotation, stacked, preferred_element_type=jnp.float32).astype(jnp.bfloat16)


def body(stored, snapshot, balance_coef, sea_mask):
    sea_float = sea_mask.astype(jnp.float32)
    mean_state = jnp.mean(stored[0].astype(jnp.float32), axis=0)
    picked = jnp.take(stored[0], snapshot[0], axis=0)
    anomaly = ((picked.astype(jnp.float32) - mean_state) * sea_float).astype(jnp.bfloat16)
    other_anomaly = from_partner(anomaly, "tm", 0)
    padded = with_halo(anomaly, (("space", 1),), 1)
    basis_now = balance(padded, balance_coef, sea_float)
    levels = lax.axis_size("tm").bit_length() - 1
    other_rims = from_partner(
        jnp.concatenate([padded[:, :1], padded[:, -1:]], axis=1), "tm", 0
    )
    other_padded = jnp.concatenate(
        [other_rims[:, :1], other_anomaly, other_rims[:, 1:]], axis=1
    )
    partner = balance(other_padded, balance_coef, sea_float)
    stacked = stack_pair(basis_now, partner)
    for level_idx in range(levels):
        if level_idx == levels - 1:
            rotation = rotation_of(stacked)
            member_share = rotation.shape[0] // lax.axis_size("tm")
            rotation = lax.dynamic_slice_in_dim(
                rotation, lax.axis_index("tm") * member_share, member_share, 0
            )
            basis_now = rotated(rotation, stacked)
        else:
            partner_stacked = from_partner(stacked, "tm", level_idx + 1)
            rotation = rotation_of(stacked)
            partner_rotation = from_partner(rotation, "tm", level_idx + 1)
            basis_now = rotated(rotation, stacked)
            partner = rotated(partner_rotation, partner_stacked)
            stacked = stack_pair(basis_now, partner)
    return basis_now.reshape(basis_now.shape[0], 3, stored.shape[2], stored.shape[3])


def solution(mesh):
    placed = (P("tm", None, "space", None), P("tm", None), P("space", None), P("space", None))
    return jax.shard_map(
        body, mesh=mesh, in_specs=placed, out_specs=P("tm", None, "space", None), check_vma=False
    )
```

```python
import jax
import jax.numpy as jnp
from jax import lax
from jax.sharding import PartitionSpec as P

inv_root2 = 0.7071067811865476


def summed_rows(shard, axis):
    count = lax.axis_size(axis)
    parts = lax.all_to_all(shard, axis, 0, 0, tiled=True)
    parts = parts.reshape(count, shard.shape[0] // count, shard.shape[1])
    own_rows = parts.astype(jnp.float32).sum(0)
    return lax.all_gather(own_rows, axis, axis=0, tiled=True)


def with_halo(cells, sides, width):
    for axis, dim in sides:
        count = lax.axis_size(axis)
        ends = count - 1
        head = lax.slice_in_dim(cells, 0, width, axis=dim)
        tail = lax.slice_in_dim(cells, cells.shape[dim] - width, cells.shape[dim], axis=dim)
        cells = jnp.concatenate(
            [
                lax.ppermute(tail, axis, [(i, (i + 1) % count) for i in range(ends)]),
                cells,
                lax.ppermute(head, axis, [((i + 1) % count, i) for i in range(ends)]),
            ],
            axis=dim,
        )
    return cells


def from_partner(shard, axis, stride):
    return lax.ppermute(shard, axis, [(i, i ^ 1 << stride) for i in range(lax.axis_size(axis))])


def balance(padded, balance_coef, sea_float):
    center = padded[:, 1:-1, :]
    cells = lax.broadcasted_iota(jnp.int32, (center.shape[2], center.shape[2]), 0)
    targets = lax.broadcasted_iota(jnp.int32, (center.shape[2], center.shape[2]), 1)
    count = center.shape[2]
    circulant = (cells == (targets + 1) % count).astype(jnp.bfloat16) - (
        cells == (targets - 1) % count
    ).astype(jnp.bfloat16)
    east_minus_west = jnp.einsum(
        "mxy,yz->mxz", center, circulant, preferred_element_type=jnp.float32
    )
    zonal_flow = (-balance_coef * sea_float * east_minus_west).astype(jnp.bfloat16)
    wide = padded.astype(jnp.float32)
    merid_flow = (balance_coef * sea_float * (wide[:, 2:, :] - wide[:, :-2, :])).astype(
        jnp.bfloat16
    )
    return jnp.stack([center, zonal_flow, merid_flow], axis=1).reshape(center.shape[0], -1)


def stack_pair(own_basis, other_basis):
    return jnp.concatenate([own_basis, other_basis], axis=0)


def rotation_of(stacked):
    members = stacked.shape[0] // 2
    local_gram = jnp.dot(stacked, stacked.T, preferred_element_type=jnp.float32)
    local_mixed = (local_gram[:, :members] + local_gram[:, members:]) * inv_root2
    mixed_cols = summed_rows(local_mixed.astype(jnp.bfloat16), "space")
    normal = jnp.dot(
        mixed_cols.T,
        mixed_cols,
        precision=lax.Precision.HIGHEST,
        preferred_element_type=jnp.float32,
    )
    half = normal.shape[0] // 2
    low_11 = jnp.linalg.cholesky(normal[:half, :half])
    low_21 = lax.linalg.triangular_solve(
        low_11, normal[half:, :half], left_side=False, lower=True, transpose_a=True
    )
    low_22 = jnp.linalg.cholesky(normal[half:, half:] - highest_dot(low_21, low_21.T))
    upper_rows = jax.scipy.linalg.solve_triangular(low_11, mixed_cols[:, :half].T, lower=True)
    lower_rows = jax.scipy.linalg.solve_triangular(
        low_22, mixed_cols[:, half:].T - highest_dot(low_21, upper_rows), lower=True
    )
    return (upper_rows * inv_root2).astype(jnp.bfloat16), (lower_rows * inv_root2).astype(
        jnp.bfloat16
    )


def highest_dot(left, right):
    return jnp.dot(
        left, right, precision=lax.Precision.HIGHEST, preferred_element_type=jnp.float32
    )


def rotated(rotation, stacked):
    return jnp.dot(rotation, stacked, preferred_element_type=jnp.float32).astype(jnp.bfloat16)


def body(stored, snapshot, balance_coef, sea_mask):
    sea_float = sea_mask.astype(jnp.float32)
    mean_state = jnp.mean(stored[0].astype(jnp.float32), axis=0)
    picked = jnp.take(stored[0], snapshot[0], axis=0)
    anomaly = ((picked.astype(jnp.float32) - mean_state) * sea_float).astype(jnp.bfloat16)
    other_anomaly = from_partner(anomaly, "tm", 0)
    padded = with_halo(anomaly, (("space", 1),), 1)
    basis_now = balance(padded, balance_coef, sea_float)
    levels = lax.axis_size("tm").bit_length() - 1
    other_rims = from_partner(
        jnp.concatenate([padded[:, :1], padded[:, -1:]], axis=1), "tm", 0
    )
    other_padded = jnp.concatenate(
        [other_rims[:, :1], other_anomaly, other_rims[:, 1:]], axis=1
    )
    partner = balance(other_padded, balance_coef, sea_float)
    stacked = stack_pair(basis_now, partner)
    for level_idx in range(levels):
        if level_idx == levels - 1:
            rotation = jnp.concatenate(rotation_of(stacked), axis=0)
            member_share = rotation.shape[0] // lax.axis_size("tm")
            rotation = lax.dynamic_slice_in_dim(
                rotation, lax.axis_index("tm") * member_share, member_share, 0
            )
            basis_now = rotated(rotation, stacked)
        else:
            partner_stacked = from_partner(stacked, "tm", level_idx + 1)
            halves = rotation_of(stacked)
            partner_upper = from_partner(halves[0], "tm", level_idx + 1)
            partner_halves = [partner_upper, from_partner(halves[1], "tm", level_idx + 1)]
            basis_now = jnp.concatenate([rotated(half, stacked) for half in halves], axis=0)
            partner = jnp.concatenate(
                [rotated(half, partner_stacked) for half in partner_halves], axis=0
            )
            stacked = stack_pair(basis_now, partner)
    return basis_now.reshape(basis_now.shape[0], 3, stored.shape[2], stored.shape[3])


def solution(mesh):
    placed = (P("tm", None, "space", None), P("tm", None), P("space", None), P("space", None))
    return jax.shard_map(
        body, mesh=mesh, in_specs=placed, out_specs=P("tm", None, "space", None),
        check_vma=False,
    )
```

```python
import jax
import jax.numpy as jnp
from jax import lax
from jax.sharding import PartitionSpec as P

inv_root2 = 0.7071067811865476


def gathered_total(shard, axis):
    return lax.all_gather(shard, axis).astype(jnp.float32).sum(0)


def summed_rows(shard, axis):
    count = lax.axis_size(axis)
    parts = lax.all_to_all(shard, axis, 0, 0, tiled=True)
    parts = parts.reshape(count, shard.shape[0] // count, shard.shape[1])
    own_rows = parts.astype(jnp.float32).sum(0)
    return lax.all_gather(own_rows, axis, axis=0, tiled=True)


def with_halo(cells, sides, width):
    for axis, dim in sides:
        count = lax.axis_size(axis)
        ends = count - 1
        head = lax.slice_in_dim(cells, 0, width, axis=dim)
        tail = lax.slice_in_dim(cells, cells.shape[dim] - width, cells.shape[dim], axis=dim)
        cells = jnp.concatenate(
            [
                lax.ppermute(tail, axis, [(i, (i + 1) % count) for i in range(ends)]),
                cells,
                lax.ppermute(head, axis, [((i + 1) % count, i) for i in range(ends)]),
            ],
            axis=dim,
        )
    return cells


def from_partner(shard, axis, stride):
    return lax.ppermute(shard, axis, [(i, i ^ 1 << stride) for i in range(lax.axis_size(axis))])


def balance(padded, balance_coef, sea_float):
    center = padded[:, 1:-1, :]
    cells = lax.broadcasted_iota(jnp.int32, (center.shape[2], center.shape[2]), 0)
    targets = lax.broadcasted_iota(jnp.int32, (center.shape[2], center.shape[2]), 1)
    count = center.shape[2]
    circulant = (cells == (targets + 1) % count).astype(jnp.bfloat16) - (
        cells == (targets - 1) % count
    ).astype(jnp.bfloat16)
    east_minus_west = jnp.einsum(
        "mxy,yz->mxz", center, circulant, preferred_element_type=jnp.float32
    )
    zonal_flow = (-balance_coef * sea_float * east_minus_west).astype(jnp.bfloat16)
    wide = padded.astype(jnp.float32)
    merid_flow = (balance_coef * sea_float * (wide[:, 2:, :] - wide[:, :-2, :])).astype(
        jnp.bfloat16
    )
    return jnp.stack([center, zonal_flow, merid_flow], axis=1).reshape(center.shape[0], -1)


def stack_pair(own_basis, other_basis):
    return jnp.concatenate([own_basis, other_basis], axis=0)


def rotation_of(stacked):
    members = stacked.shape[0] // 2
    local_gram = jnp.dot(stacked, stacked.T, preferred_element_type=jnp.float32)
    local_mixed = (local_gram[:, :members] + local_gram[:, members:]) * inv_root2
    mixed_cols = summed_rows(local_mixed.astype(jnp.bfloat16), "space")
    normal = jnp.dot(
        mixed_cols.T,
        mixed_cols,
        precision=lax.Precision.HIGHEST,
        preferred_element_type=jnp.float32,
    )
    half = normal.shape[0] // 2
    low_11 = lax.linalg.cholesky(normal[:half, :half], symmetrize_input=False)
    low_21 = lax.linalg.triangular_solve(
        low_11, normal[half:, :half], left_side=False, lower=True, transpose_a=True
    )
    low_22 = lax.linalg.cholesky(
        normal[half:, half:] - highest_dot(low_21, low_21.T), symmetrize_input=False
    )
    upper_rows = jax.scipy.linalg.solve_triangular(low_11, mixed_cols[:, :half].T, lower=True)
    lower_rows = jax.scipy.linalg.solve_triangular(
        low_22, mixed_cols[:, half:].T - highest_dot(low_21, upper_rows), lower=True
    )
    return (jnp.concatenate([upper_rows, lower_rows], axis=0) * inv_root2).astype(jnp.bfloat16)


def highest_dot(left, right):
    return jnp.dot(
        left, right, precision=lax.Precision.HIGHEST, preferred_element_type=jnp.float32
    )


def rotated(rotation, stacked):
    return jnp.dot(rotation, stacked, preferred_element_type=jnp.float32).astype(jnp.bfloat16)


def body(stored, snapshot, balance_coef, sea_mask):
    sea_float = sea_mask.astype(jnp.float32)
    mean_state = jnp.mean(stored[0].astype(jnp.float32), axis=0)
    picked = jnp.take(stored[0], snapshot[0], axis=0)
    anomaly = ((picked.astype(jnp.float32) - mean_state) * sea_float).astype(jnp.bfloat16)
    other_anomaly = from_partner(anomaly, "tm", 0)
    padded = with_halo(anomaly, (("space", 1),), 1)
    basis_now = balance(padded, balance_coef, sea_float)
    levels = lax.axis_size("tm").bit_length() - 1
    other_rims = from_partner(
        jnp.concatenate([padded[:, :1], padded[:, -1:]], axis=1), "tm", 0
    )
    other_padded = jnp.concatenate(
        [other_rims[:, :1], other_anomaly, other_rims[:, 1:]], axis=1
    )
    partner = balance(other_padded, balance_coef, sea_float)
    stacked = stack_pair(basis_now, partner)
    for level_idx in range(levels):
        if level_idx == levels - 1:
            rotation = rotation_of(stacked)
            member_share = rotation.shape[0] // lax.axis_size("tm")
            rotation = lax.dynamic_slice_in_dim(
                rotation, lax.axis_index("tm") * member_share, member_share, 0
            )
            basis_now = rotated(rotation, stacked)
        else:
            partner_stacked = from_partner(stacked, "tm", level_idx + 1)
            rotation = rotation_of(stacked)
            partner_rotation = from_partner(rotation, "tm", level_idx + 1)
            basis_now = rotated(rotation, stacked)
            partner = rotated(partner_rotation, partner_stacked)
            stacked = stack_pair(basis_now, partner)
    return basis_now.reshape(basis_now.shape[0], 3, stored.shape[2], stored.shape[3])


def solution(mesh):
    placed = (P("tm", None, "space", None), P("tm", None), P("space", None), P("space", None))
    return jax.shard_map(
        body, mesh=mesh, in_specs=placed, out_specs=P("tm", None, "space", None), check_vma=False
    )
```

```python
import jax
import jax.numpy as jnp
from jax import lax
from jax.sharding import PartitionSpec as P

inv_root2 = 0.7071067811865476


def gathered_total(shard, axis):
    return lax.all_gather(shard, axis).astype(jnp.float32).sum(0)


def summed_rows(shard, axis):
    count = lax.axis_size(axis)
    parts = lax.all_to_all(shard, axis, 0, 0, tiled=True)
    parts = parts.reshape(count, shard.shape[0] // count, shard.shape[1])
    own_rows = parts.astype(jnp.float32).sum(0)
    return lax.all_gather(own_rows, axis, axis=0, tiled=True)


def with_halo(cells, sides, width):
    for axis, dim in sides:
        count = lax.axis_size(axis)
        ends = count - 1
        head = lax.slice_in_dim(cells, 0, width, axis=dim)
        tail = lax.slice_in_dim(cells, cells.shape[dim] - width, cells.shape[dim], axis=dim)
        cells = jnp.concatenate(
            [
                lax.ppermute(tail, axis, [(i, (i + 1) % count) for i in range(ends)]),
                cells,
                lax.ppermute(head, axis, [((i + 1) % count, i) for i in range(ends)]),
            ],
            axis=dim,
        )
    return cells


def from_partner(shard, axis, stride):
    return lax.ppermute(shard, axis, [(i, i ^ 1 << stride) for i in range(lax.axis_size(axis))])


def balance(padded, balance_coef, sea_float):
    center = padded[:, 1:-1, :]
    cells = lax.broadcasted_iota(jnp.int32, (center.shape[2], center.shape[2]), 0)
    targets = lax.broadcasted_iota(jnp.int32, (center.shape[2], center.shape[2]), 1)
    count = center.shape[2]
    circulant = (cells == (targets + 1) % count).astype(jnp.bfloat16) - (
        cells == (targets - 1) % count
    ).astype(jnp.bfloat16)
    east_minus_west = jnp.einsum(
        "mxy,yz->mxz", center, circulant, preferred_element_type=jnp.float32
    )
    zonal_flow = (-balance_coef * sea_float * east_minus_west).astype(jnp.bfloat16)
    wide = padded.astype(jnp.float32)
    merid_flow = (balance_coef * sea_float * (wide[:, 2:, :] - wide[:, :-2, :])).astype(
        jnp.bfloat16
    )
    return jnp.stack([center, zonal_flow, merid_flow], axis=1).reshape(center.shape[0], -1)


def stack_pair(own_basis, other_basis):
    return jnp.concatenate([own_basis, other_basis], axis=0)


def rotation_of(own_basis, other_basis):
    own_own = jnp.dot(own_basis, own_basis.T, preferred_element_type=jnp.float32)
    own_other = jnp.dot(own_basis, other_basis.T, preferred_element_type=jnp.float32)
    other_other = jnp.dot(other_basis, other_basis.T, preferred_element_type=jnp.float32)
    local_mixed = (
        jnp.concatenate([own_own + own_other, own_other.T + other_other], axis=0) * inv_root2
    )
    mixed_cols = summed_rows(local_mixed.astype(jnp.bfloat16), "space")
    normal = jnp.dot(
        mixed_cols.T,
        mixed_cols,
        precision=lax.Precision.HIGHEST,
        preferred_element_type=jnp.float32,
    )
    half = normal.shape[0] // 2
    low_11 = lax.linalg.cholesky(normal[:half, :half], symmetrize_input=False)
    low_21 = lax.linalg.triangular_solve(
        low_11, normal[half:, :half], left_side=False, lower=True, transpose_a=True
    )
    low_22 = lax.linalg.cholesky(
        normal[half:, half:] - highest_dot(low_21, low_21.T), symmetrize_input=False
    )
    upper_rows = jax.scipy.linalg.solve_triangular(low_11, mixed_cols[:, :half].T, lower=True)
    lower_rows = jax.scipy.linalg.solve_triangular(
        low_22, mixed_cols[:, half:].T - highest_dot(low_21, upper_rows), lower=True
    )
    return (jnp.concatenate([upper_rows, lower_rows], axis=0) * inv_root2).astype(jnp.bfloat16)


def highest_dot(left, right):
    return jnp.dot(
        left, right, precision=lax.Precision.HIGHEST, preferred_element_type=jnp.float32
    )


def rotated(rotation, stacked):
    return jnp.dot(rotation, stacked, preferred_element_type=jnp.float32).astype(jnp.bfloat16)


def body(stored, snapshot, balance_coef, sea_mask):
    sea_float = sea_mask.astype(jnp.float32)
    mean_state = jnp.mean(stored[0].astype(jnp.float32), axis=0)
    picked = jnp.take(stored[0], snapshot[0], axis=0)
    anomaly = ((picked.astype(jnp.float32) - mean_state) * sea_float).astype(jnp.bfloat16)
    other_anomaly = from_partner(anomaly, "tm", 0)
    padded = with_halo(anomaly, (("space", 1),), 1)
    basis_now = balance(padded, balance_coef, sea_float)
    levels = lax.axis_size("tm").bit_length() - 1
    other_rims = from_partner(
        jnp.concatenate([padded[:, :1], padded[:, -1:]], axis=1), "tm", 0
    )
    other_padded = jnp.concatenate(
        [other_rims[:, :1], other_anomaly, other_rims[:, 1:]], axis=1
    )
    partner = balance(other_padded, balance_coef, sea_float)
    stacked = stack_pair(basis_now, partner)
    for level_idx in range(levels):
        if level_idx == levels - 1:
            rotation = rotation_of(basis_now, partner)
            member_share = rotation.shape[0] // lax.axis_size("tm")
            rotation = lax.dynamic_slice_in_dim(
                rotation, lax.axis_index("tm") * member_share, member_share, 0
            )
            basis_now = rotated(rotation, stacked)
        else:
            partner_stacked = from_partner(stacked, "tm", level_idx + 1)
            rotation = rotation_of(basis_now, partner)
            partner_rotation = from_partner(rotation, "tm", level_idx + 1)
            basis_now = rotated(rotation, stacked)
            partner = rotated(partner_rotation, partner_stacked)
            stacked = stack_pair(basis_now, partner)
    return basis_now.reshape(basis_now.shape[0], 3, stored.shape[2], stored.shape[3])


def solution(mesh):
    placed = (P("tm", None, "space", None), P("tm", None), P("space", None), P("space", None))
    return jax.shard_map(
        body, mesh=mesh, in_specs=placed, out_specs=P("tm", None, "space", None), check_vma=False
    )
```

```python
import jax
import jax.numpy as jnp
from jax import lax
from jax.sharding import PartitionSpec as P

inv_root2 = 0.7071067811865476


def gathered_total(shard, axis):
    return lax.all_gather(shard, axis).astype(jnp.float32).sum(0)


def summed_rows(shard, axis):
    count = lax.axis_size(axis)
    parts = lax.all_to_all(shard, axis, 0, 0, tiled=True)
    parts = parts.reshape(count, shard.shape[0] // count, shard.shape[1])
    own_rows = parts.astype(jnp.float32).sum(0)
    index = lax.axis_index(axis)
    step = 1
    while step < count:
        other = lax.ppermute(own_rows, axis, [(i, i ^ step) for i in range(count)])
        own_rows = jnp.where(
            index // step % 2 == 0,
            jnp.concatenate([own_rows, other], axis=0),
            jnp.concatenate([other, own_rows], axis=0),
        )
        step *= 2
    return own_rows


def with_halo(cells, sides, width):
    for axis, dim in sides:
        count = lax.axis_size(axis)
        ends = count - 1
        head = lax.slice_in_dim(cells, 0, width, axis=dim)
        tail = lax.slice_in_dim(cells, cells.shape[dim] - width, cells.shape[dim], axis=dim)
        cells = jnp.concatenate(
            [
                lax.ppermute(tail, axis, [(i, (i + 1) % count) for i in range(ends)]),
                cells,
                lax.ppermute(head, axis, [((i + 1) % count, i) for i in range(ends)]),
            ],
            axis=dim,
        )
    return cells


def from_partner(shard, axis, stride):
    return lax.ppermute(shard, axis, [(i, i ^ 1 << stride) for i in range(lax.axis_size(axis))])


def balance(padded, balance_coef, sea_float):
    center = padded[:, 1:-1, :]
    cells = lax.broadcasted_iota(jnp.int32, (center.shape[2], center.shape[2]), 0)
    targets = lax.broadcasted_iota(jnp.int32, (center.shape[2], center.shape[2]), 1)
    count = center.shape[2]
    circulant = (cells == (targets + 1) % count).astype(jnp.bfloat16) - (
        cells == (targets - 1) % count
    ).astype(jnp.bfloat16)
    east_minus_west = jnp.einsum(
        "mxy,yz->mxz", center, circulant, preferred_element_type=jnp.float32
    )
    zonal_flow = (-balance_coef * sea_float * east_minus_west).astype(jnp.bfloat16)
    wide = padded.astype(jnp.float32)
    merid_flow = (balance_coef * sea_float * (wide[:, 2:, :] - wide[:, :-2, :])).astype(
        jnp.bfloat16
    )
    return jnp.stack([center, zonal_flow, merid_flow], axis=1).reshape(center.shape[0], -1)


def stack_pair(own_basis, other_basis):
    return jnp.concatenate([own_basis, other_basis], axis=0)


def rotation_of(stacked):
    members = stacked.shape[0] // 2
    local_gram = jnp.dot(stacked, stacked.T, preferred_element_type=jnp.float32)
    local_mixed = (local_gram[:, :members] + local_gram[:, members:]) * inv_root2
    mixed_cols = summed_rows(local_mixed.astype(jnp.bfloat16), "space")
    normal = jnp.dot(
        mixed_cols.T,
        mixed_cols,
        precision=lax.Precision.HIGHEST,
        preferred_element_type=jnp.float32,
    )
    half = normal.shape[0] // 2
    low_11 = lax.linalg.cholesky(normal[:half, :half], symmetrize_input=False)
    low_21 = lax.linalg.triangular_solve(
        low_11, normal[half:, :half], left_side=False, lower=True, transpose_a=True
    )
    low_22 = lax.linalg.cholesky(
        normal[half:, half:] - highest_dot(low_21, low_21.T), symmetrize_input=False
    )
    upper_rows = jax.scipy.linalg.solve_triangular(low_11, mixed_cols[:, :half].T, lower=True)
    lower_rows = jax.scipy.linalg.solve_triangular(
        low_22, mixed_cols[:, half:].T - highest_dot(low_21, upper_rows), lower=True
    )
    return (jnp.concatenate([upper_rows, lower_rows], axis=0) * inv_root2).astype(jnp.bfloat16)


def highest_dot(left, right):
    return jnp.dot(
        left, right, precision=lax.Precision.HIGHEST, preferred_element_type=jnp.float32
    )


def rotated(rotation, stacked):
    return jnp.dot(rotation, stacked, preferred_element_type=jnp.float32).astype(jnp.bfloat16)


def body(stored, snapshot, balance_coef, sea_mask):
    sea_float = sea_mask.astype(jnp.float32)
    mean_state = jnp.mean(stored[0].astype(jnp.float32), axis=0)
    picked = jnp.take(stored[0], snapshot[0], axis=0)
    anomaly = ((picked.astype(jnp.float32) - mean_state) * sea_float).astype(jnp.bfloat16)
    other_anomaly = from_partner(anomaly, "tm", 0)
    padded = with_halo(anomaly, (("space", 1),), 1)
    basis_now = balance(padded, balance_coef, sea_float)
    levels = lax.axis_size("tm").bit_length() - 1
    other_rims = from_partner(
        jnp.concatenate([padded[:, :1], padded[:, -1:]], axis=1), "tm", 0
    )
    other_padded = jnp.concatenate(
        [other_rims[:, :1], other_anomaly, other_rims[:, 1:]], axis=1
    )
    partner = balance(other_padded, balance_coef, sea_float)
    stacked = stack_pair(basis_now, partner)
    for level_idx in range(levels):
        if level_idx == levels - 1:
            rotation = rotation_of(stacked)
            member_share = rotation.shape[0] // lax.axis_size("tm")
            rotation = lax.dynamic_slice_in_dim(
                rotation, lax.axis_index("tm") * member_share, member_share, 0
            )
            basis_now = rotated(rotation, stacked)
        else:
            partner_stacked = from_partner(stacked, "tm", level_idx + 1)
            rotation = rotation_of(stacked)
            partner_rotation = from_partner(rotation, "tm", level_idx + 1)
            basis_now = rotated(rotation, stacked)
            partner = rotated(partner_rotation, partner_stacked)
            stacked = stack_pair(basis_now, partner)
    return basis_now.reshape(basis_now.shape[0], 3, stored.shape[2], stored.shape[3])


def solution(mesh):
    placed = (P("tm", None, "space", None), P("tm", None), P("space", None), P("space", None))
    return jax.shard_map(
        body, mesh=mesh, in_specs=placed, out_specs=P("tm", None, "space", None), check_vma=False
    )
```

```python
import jax
import jax.numpy as jnp
from jax import lax
from jax.sharding import PartitionSpec as P

inv_root2 = 0.7071067811865476


def gathered_total(shard, axis):
    return lax.all_gather(shard, axis).astype(jnp.float32).sum(0)


def summed_rows(shard, axis):
    count = lax.axis_size(axis)
    parts = lax.all_to_all(shard, axis, 0, 0, tiled=True)
    parts = parts.reshape(count, shard.shape[0] // count, shard.shape[1])
    own_rows = parts.astype(jnp.float32).sum(0)
    return lax.all_gather(own_rows, axis, axis=0, tiled=True)


def with_halo(cells, sides, width):
    for axis, dim in sides:
        count = lax.axis_size(axis)
        ends = count - 1
        head = lax.slice_in_dim(cells, 0, width, axis=dim)
        tail = lax.slice_in_dim(cells, cells.shape[dim] - width, cells.shape[dim], axis=dim)
        cells = jnp.concatenate(
            [
                lax.ppermute(tail, axis, [(i, (i + 1) % count) for i in range(ends)]),
                cells,
                lax.ppermute(head, axis, [((i + 1) % count, i) for i in range(ends)]),
            ],
            axis=dim,
        )
    return cells


def from_partner(shard, axis, stride):
    return lax.ppermute(shard, axis, [(i, i ^ 1 << stride) for i in range(lax.axis_size(axis))])


def balance(padded, balance_coef, sea_float):
    center = padded[:, 1:-1, :]
    cells = lax.broadcasted_iota(jnp.int32, (center.shape[2], center.shape[2]), 0)
    targets = lax.broadcasted_iota(jnp.int32, (center.shape[2], center.shape[2]), 1)
    count = center.shape[2]
    circulant = (cells == (targets + 1) % count).astype(jnp.bfloat16) - (
        cells == (targets - 1) % count
    ).astype(jnp.bfloat16)
    east_minus_west = jnp.einsum(
        "mxy,yz->mxz", center, circulant, preferred_element_type=jnp.float32
    )
    zonal_flow = (-balance_coef * sea_float * east_minus_west).astype(jnp.bfloat16)
    wide = padded.astype(jnp.float32)
    merid_flow = (balance_coef * sea_float * (wide[:, 2:, :] - wide[:, :-2, :])).astype(
        jnp.bfloat16
    )
    return jnp.stack([center, zonal_flow, merid_flow], axis=1).reshape(center.shape[0], -1)


def stack_pair(own_basis, other_basis):
    return jnp.concatenate([own_basis, other_basis], axis=0)


def rotation_of(stacked):
    members = stacked.shape[0] // 2
    local_gram = jnp.dot(stacked, stacked.T, preferred_element_type=jnp.float32)
    local_mixed = (local_gram[:, :members] + local_gram[:, members:]) * inv_root2
    mixed_cols = summed_rows(local_mixed.astype(jnp.bfloat16), "space")
    normal = jnp.dot(
        mixed_cols.T,
        mixed_cols,
        precision=lax.Precision.HIGHEST,
        preferred_element_type=jnp.float32,
    )
    half = normal.shape[0] // 2
    low_11 = lax.linalg.cholesky(normal[:half, :half], symmetrize_input=False)
    low_21 = lax.linalg.triangular_solve(
        low_11, normal[half:, :half], left_side=False, lower=True, transpose_a=True
    )
    low_22 = lax.linalg.cholesky(
        normal[half:, half:] - highest_dot(low_21, low_21.T), symmetrize_input=False
    )
    upper_rows = jax.scipy.linalg.solve_triangular(low_11, mixed_cols[:, :half].T, lower=True)
    lower_rows = jax.scipy.linalg.solve_triangular(
        low_22, mixed_cols[:, half:].T - highest_dot(low_21, upper_rows), lower=True
    )
    return (jnp.concatenate([upper_rows, lower_rows], axis=0) * inv_root2).astype(jnp.bfloat16)


def highest_dot(left, right):
    return jnp.dot(
        left, right, precision=lax.Precision.HIGHEST, preferred_element_type=jnp.float32
    )


def rotated(rotation, stacked):
    return jnp.dot(rotation, stacked, preferred_element_type=jnp.float32).astype(jnp.bfloat16)


def body(stored, snapshot, balance_coef, sea_mask):
    sea_float = sea_mask.astype(jnp.float32)
    mean_state = jnp.mean(stored[0].astype(jnp.float32), axis=0)
    picked = jnp.take(stored[0], snapshot[0], axis=0)
    anomaly = ((picked.astype(jnp.float32) - mean_state) * sea_float).astype(jnp.bfloat16)
    other_picked = from_partner(picked, "tm", 0)
    other_mean = from_partner(mean_state, "tm", 0)
    other_anomaly = ((other_picked.astype(jnp.float32) - other_mean) * sea_float).astype(
        jnp.bfloat16
    )
    padded = with_halo(anomaly, (("space", 1),), 1)
    basis_now = balance(padded, balance_coef, sea_float)
    levels = lax.axis_size("tm").bit_length() - 1
    other_rims = from_partner(
        jnp.concatenate([padded[:, :1], padded[:, -1:]], axis=1), "tm", 0
    )
    other_padded = jnp.concatenate(
        [other_rims[:, :1], other_anomaly, other_rims[:, 1:]], axis=1
    )
    partner = balance(other_padded, balance_coef, sea_float)
    stacked = stack_pair(basis_now, partner)
    for level_idx in range(levels):
        if level_idx == levels - 1:
            rotation = rotation_of(stacked)
            member_share = rotation.shape[0] // lax.axis_size("tm")
            rotation = lax.dynamic_slice_in_dim(
                rotation, lax.axis_index("tm") * member_share, member_share, 0
            )
            basis_now = rotated(rotation, stacked)
        else:
            partner_stacked = from_partner(stacked, "tm", level_idx + 1)
            rotation = rotation_of(stacked)
            partner_rotation = from_partner(rotation, "tm", level_idx + 1)
            basis_now = rotated(rotation, stacked)
            partner = rotated(partner_rotation, partner_stacked)
            stacked = stack_pair(basis_now, partner)
    return basis_now.reshape(basis_now.shape[0], 3, stored.shape[2], stored.shape[3])


def solution(mesh):
    placed = (P("tm", None, "space", None), P("tm", None), P("space", None), P("space", None))
    return jax.shard_map(
        body, mesh=mesh, in_specs=placed, out_specs=P("tm", None, "space", None), check_vma=False
    )
```
